768 devices in a mesh: ctx: 16 (over x_hi, y), tp: 48 (over x_lo, z, core).
Axes of the slice: x: 4 (x_hi: 2, x_lo: 2; x = x_hi * 2 + x_lo), y: 8, z: 12, core: 2. Of those that a mesh axis runs over, the one named last changes fastest.
Arguments:
- projected: bfloat16 [3, 4096, 6144], P(None, 'ctx', 'tp'), may hold values from -6 to 6
- filters: float32 [384, 128], P('tp'), may hold values from -0.5 to 0.5
- out_weight: bfloat16 [6144, 6144], P('tp'), may hold values from -0.1875 to 0.1875
- grad_out: bfloat16 [4096, 6144], P('ctx', 'tp'), may hold values from -6 to 6
Outputs:
- block_out: bfloat16 [4096, 6144], P('ctx', 'tp')
- grad_inputs: bfloat16 [3, 4096, 6144], P(None, 'ctx', 'tp')
- grad_weight: float32 [6144, 6144], P('tp', 'ctx')
- grad_filters: float32 [384, 128], P('tp', 'ctx')
The draws below stay inside these ranges and needn't reach their ends.
All inputs are finite; a program needn't handle non-finite values.
Results may differ from the reference program's by a relative error of at most 0.0064.
Values may be sent and summed in bfloat16 or wider, within the bound.
No kernel may reach another device: no remote copies, remote signals or barrier semaphores. Data moves between devices by JAX's collectives and lax.ppermute only.
A program may use at most 64 MiB of HBM per device.

```python
import math
import jax
import jax.numpy as jnp
from jax import lax

CH = 6144
DM = 6144
GS = 16
K = 128
SEQ = 4096
GROUPS = 384


def with_spikes(result, own_key, source, target, shards_of, factor):
    def block_of(axis_at):
        return (jnp.arange(result.shape[axis_at]) // (result.shape[axis_at] // shards_of)).reshape((-1,) + (1,) * (result.ndim - 1 - axis_at))

    near = jax.random.permutation(own_key, shards_of)[block_of(target)]
    other_side = (block_of(target) + shards_of // 2) % shards_of
    return jnp.where((block_of(source) == near) | (block_of(source) == other_side), factor * result, result)


def block_scale(key, shape, pieces, least, high):
    loudness = 1.0
    for dim, parts in pieces:
        draws = jax.random.uniform(jax.random.fold_in(jax.random.fold_in(key, 6), dim), (parts,), jnp.float32, least / len(pieces), high / len(pieces))
        loudness = loudness * jnp.repeat(jnp.exp(draws), shape[dim] // parts).reshape((-1,) + (1,) * (len(shape) - 1 - dim))
    return loudness


def noise(rng, dims, deviation, reach, cuts=(), held_as=jnp.bfloat16):
    values = deviation * jax.random.normal(rng, dims, jnp.float32)
    if cuts:
        values = values * block_scale(rng, dims, cuts, -0.22, 0.18)
    return jnp.clip(values, -reach, reach).astype(held_as)


def heavy_noise(rng, shape, deviation, reach, shards, heavy, held_as=jnp.bfloat16):
    array = deviation * jax.random.normal(rng, shape, jnp.float32)
    if shards:
        array = array * block_scale(rng, shape, shards, -0.22, 0.18)
    return jnp.clip(with_spikes(array, jax.random.fold_in(rng, 3), *heavy), -reach, reach).astype(held_as)


def setup_inputs(seed: int = 0) -> dict:
    keys = jax.random.split(jax.random.key(seed), 5)
    projected = noise(keys[0], (3, SEQ, CH), 1.0, 6.0, ((1, 16), (2, 48)))
    filters = noise(keys[1], (GROUPS, K), K ** -0.5, 0.5, ((0, 48),), jnp.float32)
    out_weight = heavy_noise(keys[2], (CH, DM), CH ** -0.5, 0.1875, ((0, 48),), (0, 1, 48, 3.25))
    grad_out = noise(keys[3], (SEQ, DM), 1.0, 6.0, ((0, 16), (1, 48)))
    return dict(projected=projected, filters=filters, out_weight=out_weight, grad_out=grad_out)


def rounded_back(values):
    return lax.optimization_barrier(values.astype(jnp.bfloat16)).astype(jnp.float32)

def reference(projected, filters, out_weight, grad_out):
    query_rows = projected[0].astype(jnp.float32)
    key_rows = projected[1].astype(jnp.float32)
    value_rows = projected[2].astype(jnp.float32)
    tap_table = rounded_back(filters)
    per_channel = jnp.repeat(tap_table.T, GS, axis=1)
    gated_rows = rounded_back(key_rows * value_rows)
    length = gated_rows.shape[0]
    width = gated_rows.shape[1]
    padded = jnp.concatenate([jnp.zeros((K, width), jnp.float32), gated_rows], axis=0)

    def forward_step(offset, running):
        window = lax.dynamic_slice_in_dim(padded, (K - offset).astype(jnp.int32), length, 0)
        return running + per_channel[offset] * window
    filtered = lax.fori_loop(0, K, forward_step, jnp.zeros((length, width), jnp.float32))
    mixed_rows = lax.optimization_barrier((query_rows * filtered).astype(jnp.bfloat16))
    block_out = jnp.dot(mixed_rows, out_weight, preferred_element_type=jnp.float32).astype(jnp.bfloat16)
    grad_mixed = jnp.dot(grad_out, out_weight.T, preferred_element_type=jnp.float32)
    grad_filtered = rounded_back(grad_mixed * query_rows)
    grad_query = (grad_mixed * filtered).astype(jnp.bfloat16)
    ahead_rows = jnp.concatenate([grad_filtered, jnp.zeros((K, width), jnp.float32)], axis=0)

    def backward_step(offset, running):
        window = lax.dynamic_slice_in_dim(ahead_rows, jnp.asarray(offset).astype(jnp.int32), length, 0)
        return running + per_channel[offset] * window
    grad_gated = lax.fori_loop(0, K, backward_step, jnp.zeros((length, width), jnp.float32))
    grad_key = (grad_gated * value_rows).astype(jnp.bfloat16)
    grad_value = (grad_gated * key_rows).astype(jnp.bfloat16)
    grad_inputs = jnp.stack([grad_query, grad_key, grad_value])

    def filter_step(offset, tap_grads):
        window = lax.dynamic_slice_in_dim(padded, (K - offset).astype(jnp.int32), length, 0)
        tap_row = lax.optimization_barrier(jnp.sum(grad_filtered * window, axis=0))
        return lax.dynamic_update_slice_in_dim(tap_grads, tap_row[None, :], jnp.asarray(offset).astype(jnp.int32), 0)
    tap_grads = lax.fori_loop(0, K, filter_step, jnp.zeros((K, width), jnp.float32))
    grad_filters = lax.optimization_barrier(jnp.sum(tap_grads.reshape(K, GROUPS, GS), axis=2)).T / math.sqrt(SEQ * GS)
    grad_weight = jnp.dot(mixed_rows.T, grad_out, preferred_element_type=jnp.float32) / math.sqrt(SEQ)
    return (block_out, grad_inputs, grad_weight, grad_filters)
```

```python
import math

import jax
import jax.numpy as jnp
from jax import lax
from jax.sharding import Mesh, PartitionSpec as P


GATHER_BY_A2A = False


def shifted(value, axis, steps):
    count = lax.axis_size(axis)
    first, last = (max(0, -steps), min(count, count - steps))
    return lax.ppermute(value, axis, [(source, source + steps) for source in range(first, last)])


def toeplitz_blocks(tap_values, out_rows, ahead=False):
    groups, taps_count = tap_values.shape
    extent = taps_count + out_rows
    left_zeros = jnp.zeros((groups, out_rows), tap_values.dtype)
    right_zeros = jnp.zeros((groups, out_rows), tap_values.dtype)
    ordered = tap_values if ahead else tap_values[:, ::-1]
    padded = jnp.concatenate([left_zeros, ordered, right_zeros], axis=1)
    length_all = padded.shape[1]
    rolled = jnp.roll(padded, -out_rows if ahead else -(out_rows - 1), axis=1)
    tiled = jnp.tile(rolled, (1, out_rows))
    sheared = tiled[:, : out_rows * (length_all - 1)].reshape(groups, out_rows, length_all - 1)
    return sheared[:, :, :extent]


def summed_exchange(parts, axis):
    sent = parts.astype(jnp.bfloat16)
    got = lax.all_to_all(sent, axis, 0, 0)
    return jnp.sum(got.astype(jnp.float32), axis=0)


def local(projected, filters, out_weight, grad_out):
    out_rows = projected.shape[1]
    channels = projected.shape[2]
    groups, taps_count = filters.shape
    group_size = channels // groups
    extent = taps_count + out_rows
    chips = lax.axis_size("tpo")
    cores = lax.axis_size("core")
    tp_count = chips * cores
    ctx_count = lax.axis_size("ctx")
    features = out_weight.shape[1]
    query_rows = projected[0].astype(jnp.float32)
    key_rows = projected[1].astype(jnp.float32)
    value_rows = projected[2].astype(jnp.float32)
    gated_rows = (key_rows * value_rows).astype(jnp.bfloat16)
    earlier = shifted(gated_rows[out_rows - taps_count :], "ctx", 1)
    extended = jnp.concatenate([earlier, gated_rows], axis=0).reshape(extent, groups, group_size)
    taps = filters.astype(jnp.bfloat16)
    blocks = toeplitz_blocks(taps, out_rows)
    filtered = jnp.einsum(
        "gts,sgc->tgc", blocks, extended, preferred_element_type=jnp.float32
    ).reshape(out_rows, channels)
    mixed_rows = (query_rows * filtered).astype(jnp.bfloat16)
    partial_out = jnp.einsum("cd,tc->dt", out_weight, mixed_rows, preferred_element_type=jnp.float32)
    block = features // tp_count
    halves = partial_out.reshape(chips, cores, block, out_rows)
    pair = lax.all_to_all(halves, "core", 1, 1)
    chip_sum = jnp.sum(pair, axis=1)
    own_features = summed_exchange(chip_sum, "tpo")
    block_out = own_features.T.astype(jnp.bfloat16)
    if GATHER_BY_A2A:
        copies = jnp.broadcast_to(grad_out[None], (tp_count,) + grad_out.shape)
        pieces = lax.all_to_all(copies, "tp", 0, 0)
        full_grad = jnp.transpose(pieces, (1, 0, 2)).reshape(out_rows, features)
    else:
        same_core = lax.all_gather(grad_out, "tpo", axis=0)
        both = lax.all_gather(same_core, "core", axis=0)
        full_grad = jnp.transpose(both, (2, 1, 0, 3)).reshape(out_rows, features)
    block_out, full_grad = lax.optimization_barrier((block_out, full_grad))
    grad_mixed = jnp.einsum("td,cd->tc", full_grad, out_weight, preferred_element_type=jnp.float32)
    grad_filtered = (grad_mixed * query_rows).astype(jnp.bfloat16)
    grad_query = (grad_mixed * filtered).astype(jnp.bfloat16)
    following = shifted(grad_filtered[:taps_count], "ctx", -1)
    ahead_rows = jnp.concatenate([grad_filtered, following], axis=0).reshape(
        extent, groups, group_size
    )
    grad_gated = jnp.einsum(
        "gts,sgc->tgc", toeplitz_blocks(taps, out_rows, ahead=True), ahead_rows, preferred_element_type=jnp.float32
    ).reshape(out_rows, channels)
    grad_key = (grad_gated * value_rows).astype(jnp.bfloat16)
    grad_value = (grad_gated * key_rows).astype(jnp.bfloat16)
    grad_inputs = jnp.stack([grad_query, grad_key, grad_value])
    flipped = jnp.einsum(
        "tgc,sgc->gts",
        grad_filtered.reshape(out_rows, groups, group_size),
        jnp.pad(extended[::-1], ((0, 1), (0, 0), (0, 0))),
        preferred_element_type=jnp.float32,
    )
    flattened = flipped.reshape(groups, out_rows * (extent + 1))
    diagonals = flattened[:, out_rows - 1 : out_rows - 1 + out_rows * extent].reshape(
        groups, out_rows, extent
    )[:, :, :taps_count]
    sequence = ctx_count * out_rows
    filter_term = jnp.sum(diagonals, axis=1) / math.sqrt(sequence * group_size)
    weight_scale = 1.0 / math.sqrt(sequence)
    weight_term = (
        jnp.einsum("tc,td->dc", mixed_rows, full_grad, preferred_element_type=jnp.float32)
        * weight_scale
    )
    own_cols = features // ctx_count
    own_taps = taps_count // ctx_count
    weight_parts = weight_term.reshape(ctx_count, own_cols * channels)
    filter_parts = jnp.transpose(filter_term.reshape(groups, ctx_count, own_taps), (1, 0, 2)).reshape(
        ctx_count, groups * own_taps
    )
    summed = summed_exchange(jnp.concatenate([weight_parts, filter_parts], axis=1), "ctx")
    grad_weight = summed[: own_cols * channels].reshape(own_cols, channels).T
    grad_filters = summed[own_cols * channels :].reshape(groups, own_taps)
    return (block_out, grad_inputs, grad_weight, grad_filters)


def solution(mesh):
    tp_count = mesh.shape["tp"]
    split = Mesh(mesh.devices.reshape(mesh.shape["ctx"], tp_count // 2, 2), ("ctx", "tpo", "core"))
    tp = ("tpo", "core")
    placed = (P(None, "ctx", tp), P(tp, None), P(tp, None), P("ctx", tp))
    return jax.shard_map(
        local,
        mesh=split,
        in_specs=placed,
        out_specs=(P("ctx", tp), P(None, "ctx", tp), P(tp, "ctx"), P(tp, "ctx")),
        check_vma=False,
    )
```

```python
import math

import jax
import jax.numpy as jnp
from jax import lax
from jax.sharding import Mesh, PartitionSpec as P


GATHER_BY_A2A = False


def shifted(value, axis, steps):
    count = lax.axis_size(axis)
    first, last = (max(0, -steps), min(count, count - steps))
    return lax.ppermute(value, axis, [(source, source + steps) for source in range(first, last)])


def toeplitz_blocks(tap_values, out_rows, ahead=False):
    groups, taps_count = tap_values.shape
    extent = taps_count + out_rows
    left_zeros = jnp.zeros((groups, out_rows), tap_values.dtype)
    right_zeros = jnp.zeros((groups, out_rows), tap_values.dtype)
    ordered = tap_values if ahead else tap_values[:, ::-1]
    padded = jnp.concatenate([left_zeros, ordered, right_zeros], axis=1)
    length_all = padded.shape[1]
    rolled = jnp.roll(padded, -out_rows if ahead else -(out_rows - 1), axis=1)
    tiled = jnp.tile(rolled, (1, out_rows))
    sheared = tiled[:, : out_rows * (length_all - 1)].reshape(groups, out_rows, length_all - 1)
    return sheared[:, :, :extent]


def summed_exchange(parts, axis):
    sent = parts.astype(jnp.bfloat16)
    got = lax.all_to_all(sent, axis, 0, 0)
    return jnp.sum(got.astype(jnp.float32), axis=0)


def local(projected, filters, out_weight, grad_out):
    out_rows = projected.shape[1]
    channels = projected.shape[2]
    groups, taps_count = filters.shape
    group_size = channels // groups
    extent = taps_count + out_rows
    chips = lax.axis_size("tpo")
    cores = lax.axis_size("core")
    tp_count = chips * cores
    ctx_count = lax.axis_size("ctx")
    features = out_weight.shape[1]
    query_rows = projected[0].astype(jnp.float32)
    key_rows = projected[1].astype(jnp.float32)
    value_rows = projected[2].astype(jnp.float32)
    gated_rows = (key_rows * value_rows).astype(jnp.bfloat16)
    earlier = shifted(gated_rows[out_rows - taps_count :], "ctx", 1)
    extended = jnp.concatenate([earlier, gated_rows], axis=0).reshape(extent, groups, group_size)
    taps = filters.astype(jnp.bfloat16)
    blocks = toeplitz_blocks(taps, out_rows)
    filtered = jnp.einsum(
        "gts,sgc->tgc", blocks, extended, preferred_element_type=jnp.float32
    ).reshape(out_rows, channels)
    mixed_rows = (query_rows * filtered).astype(jnp.bfloat16)
    partial_out = jnp.einsum("cd,tc->dt", out_weight, mixed_rows, preferred_element_type=jnp.float32)
    block = features // tp_count
    halves = partial_out.reshape(chips, cores, block, out_rows)
    pair = lax.all_to_all(halves, "core", 1, 1)
    chip_sum = jnp.sum(pair, axis=1)
    own_features = summed_exchange(chip_sum, "tpo")
    block_out = own_features.T.astype(jnp.bfloat16)
    if GATHER_BY_A2A:
        copies = jnp.broadcast_to(grad_out[None], (tp_count,) + grad_out.shape)
        pieces = lax.all_to_all(copies, "tp", 0, 0)
        full_grad = jnp.transpose(pieces, (1, 0, 2)).reshape(out_rows, features)
    else:
        same_core = lax.all_gather(grad_out, "tpo", axis=0)
        partner = lax.ppermute(same_core, "core", [(0, 1), (1, 0)])
        first = lax.axis_index("core") == 0
        both = jnp.stack([jnp.where(first, same_core, partner), jnp.where(first, partner, same_core)], axis=2)
        full_grad = jnp.transpose(both, (1, 0, 2, 3)).reshape(out_rows, features)
    block_out, full_grad = lax.optimization_barrier((block_out, full_grad))
    grad_mixed = jnp.einsum("td,cd->tc", full_grad, out_weight, preferred_element_type=jnp.float32)
    grad_filtered = (grad_mixed * query_rows).astype(jnp.bfloat16)
    grad_query = (grad_mixed * filtered).astype(jnp.bfloat16)
    following = shifted(grad_filtered[:taps_count], "ctx", -1)
    ahead_rows = jnp.concatenate([grad_filtered, following], axis=0).reshape(
        extent, groups, group_size
    )
    grad_gated = jnp.einsum(
        "gts,sgc->tgc", toeplitz_blocks(taps, out_rows, ahead=True), ahead_rows, preferred_element_type=jnp.float32
    ).reshape(out_rows, channels)
    grad_key = (grad_gated * value_rows).astype(jnp.bfloat16)
    grad_value = (grad_gated * key_rows).astype(jnp.bfloat16)
    grad_inputs = jnp.stack([grad_query, grad_key, grad_value])
    flipped = jnp.einsum(
        "tgc,sgc->gts",
        grad_filtered.reshape(out_rows, groups, group_size),
        jnp.pad(extended[::-1], ((0, 1), (0, 0), (0, 0))),
        preferred_element_type=jnp.float32,
    )
    flattened = flipped.reshape(groups, out_rows * (extent + 1))
    diagonals = flattened[:, out_rows - 1 : out_rows - 1 + out_rows * extent].reshape(
        groups, out_rows, extent
    )[:, :, :taps_count]
    sequence = ctx_count * out_rows
    filter_term = jnp.sum(diagonals, axis=1) / math.sqrt(sequence * group_size)
    weight_scale = 1.0 / math.sqrt(sequence)
    weight_term = (
        jnp.einsum("tc,td->dc", mixed_rows, full_grad, preferred_element_type=jnp.float32)
        * weight_scale
    )
    own_cols = features // ctx_count
    own_taps = taps_count // ctx_count
    weight_parts = weight_term.reshape(ctx_count, own_cols * channels)
    filter_parts = jnp.transpose(filter_term.reshape(groups, ctx_count, own_taps), (1, 0, 2)).reshape(
        ctx_count, groups * own_taps
    )
    summed = summed_exchange(jnp.concatenate([weight_parts, filter_parts], axis=1), "ctx")
    grad_weight = summed[: own_cols * channels].reshape(own_cols, channels).T
    grad_filters = summed[own_cols * channels :].reshape(groups, own_taps)
    return (block_out, grad_inputs, grad_weight, grad_filters)


def solution(mesh):
    tp_count = mesh.shape["tp"]
    split = Mesh(mesh.devices.reshape(mesh.shape["ctx"], tp_count // 2, 2), ("ctx", "tpo", "core"))
    tp = ("tpo", "core")
    placed = (P(None, "ctx", tp), P(tp, None), P(tp, None), P("ctx", tp))
    return jax.shard_map(
        local,
        mesh=split,
        in_specs=placed,
        out_specs=(P("ctx", tp), P(None, "ctx", tp), P(tp, "ctx"), P(tp, "ctx")),
        check_vma=False,
    )
```

```python
import math

import jax
import jax.numpy as jnp
from jax import lax
from jax.sharding import Mesh, PartitionSpec as P


GATHER_BY_A2A = False


def shifted(value, axis, steps):
    count = lax.axis_size(axis)
    first, last = (max(0, -steps), min(count, count - steps))
    return lax.ppermute(value, axis, [(source, source + steps) for source in range(first, last)])


def toeplitz_blocks(tap_values, out_rows, ahead=False):
    groups, taps_count = tap_values.shape
    extent = taps_count + out_rows
    left_zeros = jnp.zeros((groups, out_rows), tap_values.dtype)
    right_zeros = jnp.zeros((groups, out_rows), tap_values.dtype)
    ordered = tap_values if ahead else tap_values[:, ::-1]
    padded = jnp.concatenate([left_zeros, ordered, right_zeros], axis=1)
    length_all = padded.shape[1]
    rolled = jnp.roll(padded, -out_rows if ahead else -(out_rows - 1), axis=1)
    tiled = jnp.tile(rolled, (1, out_rows))
    sheared = tiled[:, : out_rows * (length_all - 1)].reshape(groups, out_rows, length_all - 1)
    return sheared[:, :, :extent]


def summed_exchange(parts, axis):
    sent = parts.astype(jnp.bfloat16)
    got = lax.all_to_all(sent, axis, 0, 0)
    return jnp.sum(got.astype(jnp.float32), axis=0)


def local(projected, filters, out_weight, grad_out):
    out_rows = projected.shape[1]
    channels = projected.shape[2]
    groups, taps_count = filters.shape
    group_size = channels // groups
    extent = taps_count + out_rows
    chips = lax.axis_size("tpo")
    cores = lax.axis_size("core")
    tp_count = chips * cores
    ctx_count = lax.axis_size("ctx")
    features = out_weight.shape[1]
    query_rows = projected[0].astype(jnp.float32)
    key_rows = projected[1].astype(jnp.float32)
    value_rows = projected[2].astype(jnp.float32)
    gated_rows = (key_rows * value_rows).astype(jnp.bfloat16)
    earlier = shifted(gated_rows[out_rows - taps_count :], "ctx", 1)
    extended = jnp.concatenate([earlier, gated_rows], axis=0).reshape(extent, groups, group_size)
    taps = filters.astype(jnp.bfloat16)
    blocks = toeplitz_blocks(taps, out_rows)
    filtered = jnp.einsum(
        "gts,sgc->tgc", blocks, extended, preferred_element_type=jnp.float32
    ).reshape(out_rows, channels)
    mixed_rows = (query_rows * filtered).astype(jnp.bfloat16)
    partial_out = jnp.einsum("cd,tc->dt", out_weight, mixed_rows, preferred_element_type=jnp.float32)
    block = features // tp_count
    halves = partial_out.reshape(chips, cores, block, out_rows)
    pair = lax.all_to_all(halves, "core", 1, 1)
    chip_sum = jnp.sum(pair, axis=1)
    own_features = summed_exchange(chip_sum, "tpo")
    block_out = own_features.T.astype(jnp.bfloat16)
    if GATHER_BY_A2A:
        copies = jnp.broadcast_to(grad_out[None], (tp_count,) + grad_out.shape)
        pieces = lax.all_to_all(copies, "tp", 0, 0)
        full_grad = jnp.transpose(pieces, (1, 0, 2)).reshape(out_rows, features)
    else:
        same_core = lax.all_gather(grad_out, "tpo", axis=0)
        partner = lax.ppermute(same_core, "core", [(0, 1), (1, 0)])
        first = lax.axis_index("core") == 0
        both = jnp.stack([jnp.where(first, same_core, partner), jnp.where(first, partner, same_core)], axis=2)
        full_grad = jnp.transpose(both, (1, 0, 2, 3)).reshape(out_rows, features)
    block_out, full_grad = lax.optimization_barrier((block_out, full_grad))
    grad_mixed = jnp.einsum("td,cd->tc", full_grad, out_weight, preferred_element_type=jnp.float32)
    grad_filtered = (grad_mixed * query_rows).astype(jnp.bfloat16)
    grad_query = (grad_mixed * filtered).astype(jnp.bfloat16)
    following = shifted(grad_filtered[:taps_count], "ctx", -1)
    ahead_rows = jnp.concatenate([grad_filtered, following], axis=0).reshape(
        extent, groups, group_size
    )
    grad_gated = jnp.einsum(
        "gts,sgc->tgc", toeplitz_blocks(taps, out_rows, ahead=True), ahead_rows, preferred_element_type=jnp.float32
    ).reshape(out_rows, channels)
    flipped = jnp.einsum(
        "tgc,sgc->gts",
        grad_filtered.reshape(out_rows, groups, group_size),
        jnp.pad(extended[::-1], ((0, 1), (0, 0), (0, 0))),
        preferred_element_type=jnp.float32,
    )
    flattened = flipped.reshape(groups, out_rows * (extent + 1))
    diagonals = flattened[:, out_rows - 1 : out_rows - 1 + out_rows * extent].reshape(
        groups, out_rows, extent
    )[:, :, :taps_count]
    sequence = ctx_count * out_rows
    filter_term = jnp.sum(diagonals, axis=1) / math.sqrt(sequence * group_size)
    weight_scale = 1.0 / math.sqrt(sequence)
    weight_term = (
        jnp.einsum("tc,td->dc", mixed_rows, full_grad, preferred_element_type=jnp.float32)
        * weight_scale
    )
    own_cols = features // ctx_count
    own_taps = taps_count // ctx_count
    weight_parts = weight_term.reshape(ctx_count, own_cols, channels)
    filter_parts = jnp.transpose(filter_term.reshape(groups, ctx_count, own_taps), (1, 0, 2))
    filter_rows = jnp.pad(filter_parts, ((0, 0), (0, 0), (0, channels - own_taps)))
    packed = jnp.concatenate([weight_parts, filter_rows], axis=1)
    packed, _ = lax.optimization_barrier((packed, following))
    summed = summed_exchange(packed, "ctx")
    grad_weight = summed[:own_cols].T
    grad_filters = summed[own_cols:, :own_taps]
    grad_key = (grad_gated * value_rows).astype(jnp.bfloat16)
    grad_value = (grad_gated * key_rows).astype(jnp.bfloat16)
    grad_inputs = jnp.stack([grad_query, grad_key, grad_value])
    return (block_out, grad_inputs, grad_weight, grad_filters)


def solution(mesh):
    tp_count = mesh.shape["tp"]
    split = Mesh(mesh.devices.reshape(mesh.shape["ctx"], tp_count // 2, 2), ("ctx", "tpo", "core"))
    tp = ("tpo", "core")
    placed = (P(None, "ctx", tp), P(tp, None), P(tp, None), P("ctx", tp))
    return jax.shard_map(
        local,
        mesh=split,
        in_specs=placed,
        out_specs=(P("ctx", tp), P(None, "ctx", tp), P(tp, "ctx"), P(tp, "ctx")),
        check_vma=False,
    )
```

```python
import math

import jax
import jax.numpy as jnp
from jax import lax
from jax.sharding import Mesh, PartitionSpec as P


GATHER_BY_A2A = False


def shifted(value, axis, steps):
    count = lax.axis_size(axis)
    first, last = (max(0, -steps), min(count, count - steps))
    return lax.ppermute(value, axis, [(source, source + steps) for source in range(first, last)])


def toeplitz_blocks(tap_values, out_rows, ahead=False):
    groups, taps_count = tap_values.shape
    extent = taps_count + out_rows
    left_zeros = jnp.zeros((groups, out_rows), tap_values.dtype)
    right_zeros = jnp.zeros((groups, out_rows), tap_values.dtype)
    ordered = tap_values if ahead else tap_values[:, ::-1]
    padded = jnp.concatenate([left_zeros, ordered, right_zeros], axis=1)
    length_all = padded.shape[1]
    rolled = jnp.roll(padded, -out_rows if ahead else -(out_rows - 1), axis=1)
    tiled = jnp.tile(rolled, (1, out_rows))
    sheared = tiled[:, : out_rows * (length_all - 1)].reshape(groups, out_rows, length_all - 1)
    return sheared[:, :, :extent]


def summed_exchange(parts, axis):
    sent = parts.astype(jnp.bfloat16)
    got = lax.all_to_all(sent, axis, 0, 0)
    return jnp.sum(got.astype(jnp.float32), axis=0)


def local(projected, filters, out_weight, grad_out):
    out_rows = projected.shape[1]
    channels = projected.shape[2]
    groups, taps_count = filters.shape
    group_size = channels // groups
    extent = taps_count + out_rows
    chips = lax.axis_size("tpo")
    cores = lax.axis_size("core")
    tp_count = chips * cores
    ctx_count = lax.axis_size("ctx")
    features = out_weight.shape[1]
    query_rows = projected[0].astype(jnp.float32)
    key_rows = projected[1].astype(jnp.float32)
    value_rows = projected[2].astype(jnp.float32)
    gated_rows = (key_rows * value_rows).astype(jnp.bfloat16)
    earlier = shifted(gated_rows[out_rows - taps_count :], "ctx", 1)
    extended = jnp.concatenate([earlier, gated_rows], axis=0).reshape(extent, groups, group_size)
    taps = filters.astype(jnp.bfloat16)
    blocks = toeplitz_blocks(taps, out_rows)
    filtered = jnp.einsum(
        "gts,sgc->tgc", blocks, extended, preferred_element_type=jnp.float32
    ).reshape(out_rows, channels)
    mixed_rows = (query_rows * filtered).astype(jnp.bfloat16)
    partial_out = jnp.einsum("cd,tc->dt", out_weight, mixed_rows, preferred_element_type=jnp.float32)
    block = features // tp_count
    halves = partial_out.reshape(chips, cores, block, out_rows)
    pair = lax.all_to_all(halves, "core", 1, 1)
    chip_sum = jnp.sum(pair, axis=1)
    own_features = summed_exchange(chip_sum, "tpo")
    block_out = own_features.T.astype(jnp.bfloat16)
    if GATHER_BY_A2A:
        copies = jnp.broadcast_to(grad_out[None], (tp_count,) + grad_out.shape)
        pieces = lax.all_to_all(copies, "tp", 0, 0)
        full_grad = jnp.transpose(pieces, (1, 0, 2)).reshape(out_rows, features)
    else:
        same_core = lax.all_gather(grad_out, "tpo", axis=0)
        partner = lax.ppermute(same_core, "core", [(0, 1), (1, 0)])
        first = lax.axis_index("core") == 0
        both = jnp.stack([jnp.where(first, same_core, partner), jnp.where(first, partner, same_core)], axis=2)
        full_grad = both
    block_out, full_grad = lax.optimization_barrier((block_out, full_grad))
    weight_blocks = out_weight.reshape(channels, chips, cores, block)
    grad_mixed = jnp.einsum("jtkl,cjkl->tc", full_grad, weight_blocks, preferred_element_type=jnp.float32)
    grad_filtered = (grad_mixed * query_rows).astype(jnp.bfloat16)
    grad_query = (grad_mixed * filtered).astype(jnp.bfloat16)
    following = shifted(grad_filtered[:taps_count], "ctx", -1)
    ahead_rows = jnp.concatenate([grad_filtered, following], axis=0).reshape(
        extent, groups, group_size
    )
    grad_gated = jnp.einsum(
        "gts,sgc->tgc", toeplitz_blocks(taps, out_rows, ahead=True), ahead_rows, preferred_element_type=jnp.float32
    ).reshape(out_rows, channels)
    flipped = jnp.einsum(
        "tgc,sgc->gts",
        grad_filtered.reshape(out_rows, groups, group_size),
        jnp.pad(extended[::-1], ((0, 1), (0, 0), (0, 0))),
        preferred_element_type=jnp.float32,
    )
    flattened = flipped.reshape(groups, out_rows * (extent + 1))
    diagonals = flattened[:, out_rows - 1 : out_rows - 1 + out_rows * extent].reshape(
        groups, out_rows, extent
    )[:, :, :taps_count]
    sequence = ctx_count * out_rows
    filter_term = jnp.sum(diagonals, axis=1) / math.sqrt(sequence * group_size)
    weight_scale = 1.0 / math.sqrt(sequence)
    weight_term = (
        jnp.einsum("tc,jtkl->jklc", mixed_rows, full_grad, preferred_element_type=jnp.float32)
        * weight_scale
    )
    own_cols = features // ctx_count
    own_taps = taps_count // ctx_count
    weight_parts = weight_term.reshape(ctx_count, own_cols, channels)
    filter_parts = jnp.transpose(filter_term.reshape(groups, ctx_count, own_taps), (1, 0, 2))
    filter_rows = jnp.pad(filter_parts, ((0, 0), (0, 0), (0, channels - own_taps)))
    packed = jnp.concatenate([weight_parts, filter_rows], axis=1)
    packed, _ = lax.optimization_barrier((packed, following))
    summed = summed_exchange(packed, "ctx")
    grad_weight = summed[:own_cols].T
    grad_filters = summed[own_cols:, :own_taps]
    grad_key = (grad_gated * value_rows).astype(jnp.bfloat16)
    grad_value = (grad_gated * key_rows).astype(jnp.bfloat16)
    grad_inputs = jnp.stack([grad_query, grad_key, grad_value])
    return (block_out, grad_inputs, grad_weight, grad_filters)


def solution(mesh):
    tp_count = mesh.shape["tp"]
    split = Mesh(mesh.devices.reshape(mesh.shape["ctx"], tp_count // 2, 2), ("ctx", "tpo", "core"))
    tp = ("tpo", "core")
    placed = (P(None, "ctx", tp), P(tp, None), P(tp, None), P("ctx", tp))
    return jax.shard_map(
        local,
        mesh=split,
        in_specs=placed,
        out_specs=(P("ctx", tp), P(None, "ctx", tp), P(tp, "ctx"), P(tp, "ctx")),
        check_vma=False,
    )
```

```python
import math

import jax
import jax.numpy as jnp
from jax import lax
from jax.sharding import Mesh, PartitionSpec as P


GATHER_BY_A2A = False


def shifted(value, axis, steps):
    count = lax.axis_size(axis)
    first, last = (max(0, -steps), min(count, count - steps))
    return lax.ppermute(value, axis, [(source, source + steps) for source in range(first, last)])


def toeplitz_blocks(tap_values, out_rows, ahead=False):
    groups, taps_count = tap_values.shape
    extent = taps_count + out_rows
    left_zeros = jnp.zeros((groups, out_rows), tap_values.dtype)
    right_zeros = jnp.zeros((groups, out_rows), tap_values.dtype)
    ordered = tap_values if ahead else tap_values[:, ::-1]
    padded = jnp.concatenate([left_zeros, ordered, right_zeros], axis=1)
    length_all = padded.shape[1]
    rolled = jnp.roll(padded, -out_rows if ahead else -(out_rows - 1), axis=1)
    tiled = jnp.tile(rolled, (1, out_rows))
    sheared = tiled[:, : out_rows * (length_all - 1)].reshape(groups, out_rows, length_all - 1)
    return sheared[:, :, :extent]


def summed_exchange(parts, axis):
    sent = parts.astype(jnp.bfloat16)
    got = lax.all_to_all(sent, axis, 0, 0)
    return jnp.sum(got.astype(jnp.float32), axis=0)


def local(projected, filters, out_weight, grad_out):
    out_rows = projected.shape[1]
    channels = projected.shape[2]
    groups, taps_count = filters.shape
    group_size = channels // groups
    extent = taps_count + out_rows
    chips = lax.axis_size("tpo")
    cores = lax.axis_size("core")
    tp_count = chips * cores
    ctx_count = lax.axis_size("ctx")
    features = out_weight.shape[1]
    query_rows = projected[0].astype(jnp.float32)
    key_rows = projected[1].astype(jnp.float32)
    value_rows = projected[2].astype(jnp.float32)
    gated_rows = (key_rows * value_rows).astype(jnp.bfloat16)
    earlier = shifted(gated_rows[out_rows - taps_count :], "ctx", 1)
    extended = jnp.concatenate([earlier, gated_rows], axis=0).reshape(extent, groups, group_size)
    taps = filters.astype(jnp.bfloat16)
    blocks = toeplitz_blocks(taps, out_rows)
    filtered = jnp.einsum(
        "gts,sgc->tgc", blocks, extended, preferred_element_type=jnp.float32
    ).reshape(out_rows, channels)
    mixed_rows = (query_rows * filtered).astype(jnp.bfloat16)
    block = features // tp_count
    weight_blocks = out_weight.reshape(channels, chips, cores, block)
    halves = jnp.einsum("cjkl,tc->kjlt", weight_blocks, mixed_rows, preferred_element_type=jnp.float32)
    pair = lax.all_to_all(halves, "core", 0, 0)
    chip_sum = jnp.sum(pair, axis=0)
    own_features = summed_exchange(chip_sum, "tpo")
    block_out = own_features.T.astype(jnp.bfloat16)
    if GATHER_BY_A2A:
        copies = jnp.broadcast_to(grad_out[None], (tp_count,) + grad_out.shape)
        pieces = lax.all_to_all(copies, "tp", 0, 0)
        full_grad = jnp.transpose(pieces, (1, 0, 2)).reshape(out_rows, features)
    else:
        same_core = lax.all_gather(grad_out, "tpo", axis=0)
        partner = lax.ppermute(same_core, "core", [(0, 1), (1, 0)])
        first = lax.axis_index("core") == 0
        both = jnp.stack([jnp.where(first, same_core, partner), jnp.where(first, partner, same_core)], axis=2)
        full_grad = both
    block_out, full_grad = lax.optimization_barrier((block_out, full_grad))
    grad_mixed = jnp.einsum("jtkl,cjkl->tc", full_grad, weight_blocks, preferred_element_type=jnp.float32)
    grad_filtered = (grad_mixed * query_rows).astype(jnp.bfloat16)
    grad_query = (grad_mixed * filtered).astype(jnp.bfloat16)
    following = shifted(grad_filtered[:taps_count], "ctx", -1)
    ahead_rows = jnp.concatenate([grad_filtered, following], axis=0).reshape(
        extent, groups, group_size
    )
    grad_gated = jnp.einsum(
        "gts,sgc->tgc", toeplitz_blocks(taps, out_rows, ahead=True), ahead_rows, preferred_element_type=jnp.float32
    ).reshape(out_rows, channels)
    flipped = jnp.einsum(
        "tgc,sgc->gts",
        grad_filtered.reshape(out_rows, groups, group_size),
        jnp.pad(extended[::-1], ((0, 1), (0, 0), (0, 0))),
        preferred_element_type=jnp.float32,
    )
    flattened = flipped.reshape(groups, out_rows * (extent + 1))
    diagonals = flattened[:, out_rows - 1 : out_rows - 1 + out_rows * extent].reshape(
        groups, out_rows, extent
    )[:, :, :taps_count]
    sequence = ctx_count * out_rows
    filter_term = jnp.sum(diagonals, axis=1) / math.sqrt(sequence * group_size)
    weight_scale = 1.0 / math.sqrt(sequence)
    weight_term = (
        jnp.einsum("tc,jtkl->jklc", mixed_rows, full_grad, preferred_element_type=jnp.float32)
        * weight_scale
    )
    own_cols = features // ctx_count
    own_taps = taps_count // ctx_count
    weight_parts = weight_term.reshape(ctx_count, own_cols, channels)
    filter_parts = jnp.transpose(filter_term.reshape(groups, ctx_count, own_taps), (1, 0, 2))
    filter_rows = jnp.pad(filter_parts, ((0, 0), (0, 0), (0, channels - own_taps)))
    packed = jnp.concatenate([weight_parts, filter_rows], axis=1)
    packed, _ = lax.optimization_barrier((packed, following))
    summed = summed_exchange(packed, "ctx")
    grad_weight = summed[:own_cols].T
    grad_filters = summed[own_cols:, :own_taps]
    grad_key = (grad_gated * value_rows).astype(jnp.bfloat16)
    grad_value = (grad_gated * key_rows).astype(jnp.bfloat16)
    grad_inputs = jnp.stack([grad_query, grad_key, grad_value])
    return (block_out, grad_inputs, grad_weight, grad_filters)


def solution(mesh):
    tp_count = mesh.shape["tp"]
    split = Mesh(mesh.devices.reshape(mesh.shape["ctx"], tp_count // 2, 2), ("ctx", "tpo", "core"))
    tp = ("tpo", "core")
    placed = (P(None, "ctx", tp), P(tp, None), P(tp, None), P("ctx", tp))
    return jax.shard_map(
        local,
        mesh=split,
        in_specs=placed,
        out_specs=(P("ctx", tp), P(None, "ctx", tp), P(tp, "ctx"), P(tp, "ctx")),
        check_vma=False,
    )
```
